32 devices in a mesh: shift: 4 (over y, x), rows: 8 (over z, core).
Axes of the slice: x: 2, y: 2, z: 4, core: 2. Of those that a mesh axis runs over, the one named last changes fastest.
Arguments:
- filtered: bfloat16 [4, 131072, 256], P('shift', 'rows'), as said below
- weights: float32 [4, 256], P('shift'), may hold values from 0.25 to 2
Outputs:
- basis: float32 [131072, 256], P(('rows', 'shift'))
- r_factor: float32 [256, 256], replicated
The draws below stay inside these ranges and needn't reach their ends.
Inputs may be any that keep to these rules, and one draw needn't show every extreme that they name: Each filtered block is of full rank.
All inputs are finite; a program needn't handle non-finite values.
Results may differ from the reference program's by a relative error of at most 0.0003.
Values sent between devices are 32-bit elements; how exact they have to be, the bound alone decides.
No kernel may reach another device: no remote copies, remote signals or barrier semaphores. Data moves between devices by JAX's collectives and lax.ppermute only.
A program may use at most 128 MiB of HBM per device.

```python
import math
import jax
import jax.numpy as jnp
from jax import lax

K = 256
SHIFTS = 4
NROWS = 131072


def draw_filtered(key, part):
    key_vals = jax.random.fold_in(key, 0)
    key_rows = jax.random.fold_in(key, 1)
    key_shared = jax.random.fold_in(key, 3)
    values = jax.random.normal(key_vals, (SHIFTS, NROWS, K), jnp.float32)
    column_shared = jax.random.normal(key_shared, (SHIFTS, NROWS, 1), jnp.float32)
    row_scale = jnp.exp(jax.random.uniform(key_rows, (SHIFTS, NROWS, 1), jnp.float32) * jnp.log(10.0))
    values = 0.6 * values + 0.8 * column_shared
    return (values * row_scale).astype(jnp.bfloat16)


def block_levels(stream_key, extent, cuts, low, high):
    factor_of, own = 1.0, jax.random.fold_in(stream_key, 6)
    for position, parts in cuts:
        draws = jnp.exp(jax.random.uniform(jax.random.fold_in(own, position), (parts,), jnp.float32, low / len(cuts), high / len(cuts)))
        factor_of = factor_of * jnp.repeat(draws, extent[position] // parts).reshape([-1 if axis == position else 1 for axis in range(len(extent))])
    return factor_of


def setup_inputs(seed: int = 0) -> dict:
    key_of = jax.random.split(jax.random.key(seed), 3)
    filtered = draw_filtered(jax.random.fold_in(key_of[2], 71), 0)
    weights = jnp.clip(jnp.exp(math.log(2.0) - 2.0794415 * jax.random.uniform(key_of[1], (SHIFTS, K), jnp.float32) ** block_levels(key_of[1], (SHIFTS, K), ((0, 4),), -0.2, 0.2)), 0.25, 2.0)
    return {"filtered": filtered, "weights": weights}


def reference(filtered, weights):
    mixed = jnp.zeros((filtered.shape[1], filtered.shape[2]), jnp.float32)
    for shift_index in range(SHIFTS):
        mixed = mixed + weights[shift_index][None, :] * filtered[shift_index].astype(jnp.float32)
    gram = jnp.dot(mixed.T.astype(jnp.float32), mixed.astype(jnp.float32), precision=lax.Precision.HIGHEST, preferred_element_type=jnp.float32) / NROWS
    lower = jnp.linalg.cholesky(gram)
    basis = jax.scipy.linalg.solve_triangular(lower, mixed.T, lower=True).T
    return (basis, lower.T)
```

```python
import jax
import jax.numpy as jnp
from jax import lax
from jax.sharding import PartitionSpec as P


def cross_products(left, right):
    return jnp.dot(
        left.T, right, precision=lax.Precision.HIGHEST, preferred_element_type=jnp.float32
    )


def butterfly_sum(x, axes):
    size = lax.axis_size(axes)
    bit = 1
    while bit < size:
        pairs = [(i, i ^ bit) for i in range(size)]
        x = x + lax.ppermute(x, axes, pairs)
        bit *= 2
    return x


def shards(filtered, weights):
    weighted = filtered[0].astype(jnp.float32) * weights[0][None, :]
    mixed = lax.psum_scatter(weighted, "shift", scatter_dimension=0, tiled=True)
    devices_all = lax.axis_size(("shift", "rows"))
    total_rows = mixed.shape[0] * devices_all
    gram = cross_products(mixed, mixed) / total_rows
    lower = jnp.linalg.cholesky(butterfly_sum(gram, ("shift", "rows")))
    basis = jax.scipy.linalg.solve_triangular(lower, mixed.T, lower=True).T
    return (basis, lower.T)


def solution(mesh):
    in_specs = (P("shift", "rows", None), P("shift", None))
    out_specs = (P(("rows", "shift"), None), P())
    return jax.shard_map(shards, mesh=mesh, in_specs=in_specs, out_specs=out_specs, check_vma=False)
```

```python
import jax
import jax.numpy as jnp
from jax import lax
from jax.experimental import pallas as pl
from jax.experimental.pallas import tpu as pltpu
from jax.sharding import PartitionSpec as P

HIGHEST = lax.Precision.HIGHEST


def cross_products(left, right):
    return jnp.dot(left.T, right, precision=HIGHEST, preferred_element_type=jnp.float32)


def butterfly_sum(x, axes):
    size = lax.axis_size(axes)
    bit = 1
    while bit < size:
        pairs = [(i, i ^ bit) for i in range(size)]
        x = x + lax.ppermute(x, axes, pairs)
        bit *= 2
    return x


def dot(a, b):
    return jnp.dot(a, b, precision=HIGHEST, preferred_element_type=jnp.float32)


def leaf_factor(a, work):
    n = a.shape[0]
    rows = lax.broadcasted_iota(jnp.int32, (n, 2 * n), 0)
    cols = lax.broadcasted_iota(jnp.int32, (n, 2 * n), 1)
    work[...] = jnp.where(cols < n, jnp.concatenate([a, a], axis=1), (cols - n == rows).astype(jnp.float32))
    row_index = lax.broadcasted_iota(jnp.int32, (n, 1), 0)
    lane_index = lax.broadcasted_iota(jnp.int32, (1, n), 1)

    def step(j, carry):
        row = work[pl.ds(j, 1), :]
        pivot = jnp.sum(jnp.where(lane_index == j, row[:, :n], 0.0), axis=1, keepdims=True)
        scale = 1.0 / jnp.sqrt(pivot)
        scaled = row * scale
        current = work[...]
        column = jnp.sum(jnp.where(lane_index == j, current[:, :n], 0.0), axis=1, keepdims=True)
        coef = jnp.where(row_index > j, column * scale, 0.0)
        work[...] = current - coef * scaled
        work[pl.ds(j, 1), :] = scaled
        return carry

    lax.fori_loop(0, n, step, 0)
    result = work[...]
    upper = jnp.where(cols[:, :n] >= rows[:, :n], result[:, :n], 0.0)
    return upper, result[:, n:]


def factor_kernel(gram_ref, r_ref, rinv_ref, work):
    n = gram_ref.shape[0]
    h = n // 2
    g = gram_ref[...]
    r11, l11i = leaf_factor(g[:h, :h], work)
    r12 = dot(l11i, g[:h, h:])
    schur = g[h:, h:] - dot(r12.T, r12)
    r22, l22i = leaf_factor(schur, work)
    r11i = l11i.T
    r22i = l22i.T
    rinv12 = -dot(dot(r11i, r12), r22i)
    zero = jnp.zeros((h, h), jnp.float32)
    r_ref[:h, :h] = r11
    r_ref[:h, h:] = r12
    r_ref[h:, :h] = zero
    r_ref[h:, h:] = r22
    rinv_ref[:h, :h] = r11i
    rinv_ref[:h, h:] = rinv12
    rinv_ref[h:, :h] = zero
    rinv_ref[h:, h:] = r22i


def factor(gram):
    n = gram.shape[0]
    vmem = pl.BlockSpec(memory_space=pltpu.VMEM)
    return pl.pallas_call(
        factor_kernel,
        out_shape=(jax.ShapeDtypeStruct((n, n), jnp.float32), jax.ShapeDtypeStruct((n, n), jnp.float32)),
        in_specs=[vmem],
        out_specs=(vmem, vmem),
        scratch_shapes=[pltpu.VMEM((n // 2, n), jnp.float32)],
    )(gram)


def shards(filtered, weights):
    weighted = filtered[0].astype(jnp.float32) * weights[0][None, :]
    mixed = lax.psum_scatter(weighted, "shift", scatter_dimension=0, tiled=True)
    devices_all = lax.axis_size(("shift", "rows"))
    total_rows = mixed.shape[0] * devices_all
    gram = cross_products(mixed, mixed) / total_rows
    upper, upper_inv = factor(butterfly_sum(gram, ("shift", "rows")))
    basis = dot(mixed, upper_inv)
    return (basis, upper)


def solution(mesh):
    in_specs = (P("shift", "rows", None), P("shift", None))
    out_specs = (P(("rows", "shift"), None), P())
    return jax.shard_map(shards, mesh=mesh, in_specs=in_specs, out_specs=out_specs, check_vma=False)
```

```python
import jax
import jax.numpy as jnp
from jax import lax
from jax.experimental import pallas as pl
from jax.experimental.pallas import tpu as pltpu
from jax.sharding import PartitionSpec as P

HIGHEST = lax.Precision.HIGHEST


def cross_products(left, right):
    return jnp.dot(left.T, right, precision=lax.Precision.HIGH, preferred_element_type=jnp.float32)


def dot_high(a, b):
    return jnp.dot(a, b, precision=lax.Precision.HIGH, preferred_element_type=jnp.float32)


def butterfly_sum(x, axes):
    size = lax.axis_size(axes)
    bit = 1
    while bit < size:
        pairs = [(i, i ^ bit) for i in range(size)]
        x = x + lax.ppermute(x, axes, pairs)
        bit *= 2
    return x


def dot(a, b):
    return jnp.dot(a, b, precision=HIGHEST, preferred_element_type=jnp.float32)


def leaf_factor(a, work):
    n = a.shape[0]
    rows = lax.broadcasted_iota(jnp.int32, (n, 2 * n), 0)
    cols = lax.broadcasted_iota(jnp.int32, (n, 2 * n), 1)
    work[...] = jnp.where(cols < n, jnp.concatenate([a, a], axis=1), (cols - n == rows).astype(jnp.float32))
    row_index = lax.broadcasted_iota(jnp.int32, (n, 1), 0)
    lane_index = lax.broadcasted_iota(jnp.int32, (1, n), 1)

    def step(j, carry):
        row = work[pl.ds(j, 1), :]
        pivot = jnp.sum(jnp.where(lane_index == j, row[:, :n], 0.0), axis=1, keepdims=True)
        scale = 1.0 / jnp.sqrt(pivot)
        scaled = row * scale
        current = work[...]
        column = jnp.sum(jnp.where(lane_index == j, current[:, :n], 0.0), axis=1, keepdims=True)
        coef = jnp.where(row_index > j, column * scale, 0.0)
        work[...] = current - coef * scaled
        work[pl.ds(j, 1), :] = scaled
        return carry

    lax.fori_loop(0, n, step, 0)
    result = work[...]
    upper = jnp.where(cols[:, :n] >= rows[:, :n], result[:, :n], 0.0)
    return upper, result[:, n:]


def factor_kernel(gram_ref, r_ref, rinv_ref, work):
    n = gram_ref.shape[0]
    h = n // 2
    g = gram_ref[...]
    r11, l11i = leaf_factor(g[:h, :h], work)
    r12 = dot(l11i, g[:h, h:])
    schur = g[h:, h:] - dot(r12.T, r12)
    r22, l22i = leaf_factor(schur, work)
    r11i = l11i.T
    r22i = l22i.T
    rinv12 = -dot(dot(r11i, r12), r22i)
    zero = jnp.zeros((h, h), jnp.float32)
    r_ref[:h, :h] = r11
    r_ref[:h, h:] = r12
    r_ref[h:, :h] = zero
    r_ref[h:, h:] = r22
    rinv_ref[:h, :h] = r11i
    rinv_ref[:h, h:] = rinv12
    rinv_ref[h:, :h] = zero
    rinv_ref[h:, h:] = r22i


def factor(gram):
    n = gram.shape[0]
    vmem = pl.BlockSpec(memory_space=pltpu.VMEM)
    return pl.pallas_call(
        factor_kernel,
        out_shape=(jax.ShapeDtypeStruct((n, n), jnp.float32), jax.ShapeDtypeStruct((n, n), jnp.float32)),
        in_specs=[vmem],
        out_specs=(vmem, vmem),
        scratch_shapes=[pltpu.VMEM((n // 2, n), jnp.float32)],
    )(gram)


PIECES = 2


def shards(filtered, weights):
    shifts = lax.axis_size("shift")
    rows, width = filtered.shape[1], filtered.shape[2]
    block = rows // shifts
    blocks = filtered[0].reshape(shifts, PIECES, block // PIECES, width)
    mixed_pieces = []
    gram = None
    for piece in range(PIECES):
        weighted = blocks[:, piece].reshape(rows // PIECES, width).astype(jnp.float32) * weights[0][None, :]
        mixed_piece = lax.psum_scatter(weighted, "shift", scatter_dimension=0, tiled=True)
        mixed_pieces.append(mixed_piece)
        part = cross_products(mixed_piece, mixed_piece)
        gram = part if gram is None else gram + part
    mixed = jnp.concatenate(mixed_pieces, axis=0)
    devices_all = lax.axis_size(("shift", "rows"))
    total_rows = mixed.shape[0] * devices_all
    upper, upper_inv = factor(butterfly_sum(gram / total_rows, ("shift", "rows")))
    basis = dot_high(mixed, upper_inv)
    return (basis, upper)


def solution(mesh):
    in_specs = (P("shift", "rows", None), P("shift", None))
    out_specs = (P(("rows", "shift"), None), P())
    return jax.shard_map(shards, mesh=mesh, in_specs=in_specs, out_specs=out_specs, check_vma=False)
```

```python
import jax
import jax.numpy as jnp
from jax import lax
from jax.experimental import pallas as pl
from jax.experimental.pallas import tpu as pltpu
from jax.sharding import PartitionSpec as P

HIGHEST = lax.Precision.HIGHEST


def cross_products(left, right):
    return jnp.dot(left.T, right, precision=lax.Precision.HIGH, preferred_element_type=jnp.float32)


def dot_high(a, b):
    return jnp.dot(a, b, precision=lax.Precision.HIGH, preferred_element_type=jnp.float32)


def butterfly_sum(x, axes):
    size = lax.axis_size(axes)
    bit = 1
    while bit < size:
        pairs = [(i, i ^ bit) for i in range(size)]
        x = x + lax.ppermute(x, axes, pairs)
        bit *= 2
    return x


def dot(a, b):
    return jnp.dot(a, b, precision=HIGHEST, preferred_element_type=jnp.float32)


def leaf_factor(a, work):
    n = a.shape[0]
    rows = lax.broadcasted_iota(jnp.int32, (n, 2 * n), 0)
    cols = lax.broadcasted_iota(jnp.int32, (n, 2 * n), 1)
    work[...] = jnp.where(cols < n, jnp.concatenate([a, a], axis=1), (cols - n == rows).astype(jnp.float32))
    row_index = lax.broadcasted_iota(jnp.int32, (n, 1), 0)
    lane_index = lax.broadcasted_iota(jnp.int32, (1, n), 1)

    def step(j, carry):
        row = work[pl.ds(j, 1), :]
        pivot = jnp.sum(jnp.where(lane_index == j, row[:, :n], 0.0), axis=1, keepdims=True)
        scale = 1.0 / jnp.sqrt(pivot)
        scaled = row * scale
        current = work[...]
        column = jnp.sum(jnp.where(lane_index == j, current[:, :n], 0.0), axis=1, keepdims=True)
        coef = jnp.where(row_index > j, column * scale, 0.0)
        work[...] = current - coef * scaled
        work[pl.ds(j, 1), :] = scaled
        return carry

    lax.fori_loop(0, n, step, 0)
    result = work[...]
    upper = jnp.where(cols[:, :n] >= rows[:, :n], result[:, :n], 0.0)
    return upper, result[:, n:]


def factor_kernel(gram_ref, r_ref, rinv_ref, work):
    n = gram_ref.shape[0]
    h = n // 2
    g = gram_ref[...]
    r11, l11i = leaf_factor(g[:h, :h], work)
    r12 = dot(l11i, g[:h, h:])
    schur = g[h:, h:] - dot(r12.T, r12)
    r22, l22i = leaf_factor(schur, work)
    r11i = l11i.T
    r22i = l22i.T
    rinv12 = -dot(dot(r11i, r12), r22i)
    zero = jnp.zeros((h, h), jnp.float32)
    r_ref[:h, :h] = r11
    r_ref[:h, h:] = r12
    r_ref[h:, :h] = zero
    r_ref[h:, h:] = r22
    rinv_ref[:h, :h] = r11i
    rinv_ref[:h, h:] = rinv12
    rinv_ref[h:, :h] = zero
    rinv_ref[h:, h:] = r22i


def factor(gram):
    n = gram.shape[0]
    vmem = pl.BlockSpec(memory_space=pltpu.VMEM)
    return pl.pallas_call(
        factor_kernel,
        out_shape=(jax.ShapeDtypeStruct((n, n), jnp.float32), jax.ShapeDtypeStruct((n, n), jnp.float32)),
        in_specs=[vmem],
        out_specs=(vmem, vmem),
        scratch_shapes=[pltpu.VMEM((n // 2, n), jnp.float32)],
    )(gram)


def shards(filtered, weights):
    weighted = filtered[0].astype(jnp.float32) * weights[0][None, :]
    mixed = lax.psum_scatter(weighted, "shift", scatter_dimension=0, tiled=True)
    devices_all = lax.axis_size(("shift", "rows"))
    total_rows = mixed.shape[0] * devices_all
    gram = cross_products(mixed, mixed) / total_rows
    upper, upper_inv = factor(butterfly_sum(gram, ("shift", "rows")))
    basis = dot_high(mixed, upper_inv)
    return (basis, upper)


def solution(mesh):
    in_specs = (P("shift", "rows", None), P("shift", None))
    out_specs = (P(("rows", "shift"), None), P())
    return jax.shard_map(shards, mesh=mesh, in_specs=in_specs, out_specs=out_specs, check_vma=False)
```

```python
import jax
import jax.numpy as jnp
from jax import lax
from jax.experimental import pallas as pl
from jax.experimental.pallas import tpu as pltpu
from jax.sharding import PartitionSpec as P

HIGHEST = lax.Precision.HIGHEST


def cross_products(left, right):
    return jnp.dot(left.T, right, precision=lax.Precision.HIGH, preferred_element_type=jnp.float32)


def dot_high(a, b):
    return jnp.dot(a, b, precision=lax.Precision.HIGH, preferred_element_type=jnp.float32)


def butterfly_sum(x, axes):
    size = lax.axis_size(axes)
    bit = 1
    while bit < size:
        pairs = [(i, i ^ bit) for i in range(size)]
        x = x + lax.ppermute(x, axes, pairs)
        bit *= 2
    return x


def dot(a, b):
    return jnp.dot(a, b, precision=HIGHEST, preferred_element_type=jnp.float32)


def leaf_factor(a, work):
    m, width = a.shape
    rows = lax.broadcasted_iota(jnp.int32, (m, width), 0)
    cols = lax.broadcasted_iota(jnp.int32, (m, width), 1)
    work[...] = jnp.where(cols < m, a, (cols - m == rows).astype(jnp.float32))
    row_index = lax.broadcasted_iota(jnp.int32, (m, 1), 0)
    lane_index = lax.broadcasted_iota(jnp.int32, (1, width), 1)

    def step(j, carry):
        row = work[pl.ds(j, 1), :]
        pivot = jnp.sum(jnp.where(lane_index == j, row, 0.0), axis=1, keepdims=True)
        scale = 1.0 / jnp.sqrt(pivot)
        scaled = row * scale
        current = work[...]
        column = jnp.sum(jnp.where(lane_index == j, current, 0.0), axis=1, keepdims=True)
        coef = jnp.where(row_index > j, column * scale, 0.0)
        work[...] = current - coef * scaled
        work[pl.ds(j, 1), :] = scaled
        return carry

    lax.fori_loop(0, m, step, 0)
    result = work[...]
    upper = jnp.where((cols >= rows) & (cols < m), result, 0.0)
    inverse = jnp.where(cols >= m, result, 0.0)
    return upper, inverse


def factor_half(x, work):
    n = x.shape[0]
    m = n // 2
    cols = lax.broadcasted_iota(jnp.int32, (m, n), 1)
    zeros = jnp.zeros((m, n), jnp.float32)
    r11, l11i_high = leaf_factor(x[:m, :], work)
    l11i = pltpu.roll(l11i_high, m, 1)
    r12 = jnp.where(cols >= m, dot(l11i, x), 0.0)
    r12_full = jnp.concatenate([r12, zeros], axis=0)
    schur_rows = (x - dot(r12_full.T, r12_full))[m:, :]
    r22, l22i_high = leaf_factor(pltpu.roll(schur_rows, m, 1), work)
    upper = jnp.concatenate([r11 + r12, pltpu.roll(r22, m, 1)], axis=0)
    first = jnp.concatenate([l11i, zeros], axis=0)
    second = jnp.concatenate([zeros, l22i_high], axis=0)
    inverse = first + second - dot(dot(second, r12_full.T), first)
    return upper, inverse


def factor_kernel(gram_ref, r_ref, rinv_ref, work):
    n = gram_ref.shape[0]
    h = n // 2
    g = gram_ref[...]
    r11, l11i = factor_half(g[:h, :h], work)
    r12 = dot(l11i, g[:h, h:])
    schur = g[h:, h:] - dot(r12.T, r12)
    r22, l22i = factor_half(schur, work)
    r11i = l11i.T
    r22i = l22i.T
    rinv12 = -dot(dot(r11i, r12), r22i)
    zero = jnp.zeros((h, h), jnp.float32)
    r_ref[:h, :h] = r11
    r_ref[:h, h:] = r12
    r_ref[h:, :h] = zero
    r_ref[h:, h:] = r22
    rinv_ref[:h, :h] = r11i
    rinv_ref[:h, h:] = rinv12
    rinv_ref[h:, :h] = zero
    rinv_ref[h:, h:] = r22i


def factor(gram):
    n = gram.shape[0]
    vmem = pl.BlockSpec(memory_space=pltpu.VMEM)
    return pl.pallas_call(
        factor_kernel,
        out_shape=(jax.ShapeDtypeStruct((n, n), jnp.float32), jax.ShapeDtypeStruct((n, n), jnp.float32)),
        in_specs=[vmem],
        out_specs=(vmem, vmem),
        scratch_shapes=[pltpu.VMEM((n // 4, n // 2), jnp.float32)],
    )(gram)


def shards(filtered, weights):
    weighted = filtered[0].astype(jnp.float32) * weights[0][None, :]
    mixed = lax.psum_scatter(weighted, "shift", scatter_dimension=0, tiled=True)
    devices_all = lax.axis_size(("shift", "rows"))
    total_rows = mixed.shape[0] * devices_all
    gram = cross_products(mixed, mixed) / total_rows
    upper, upper_inv = factor(butterfly_sum(gram, ("shift", "rows")))
    basis = dot_high(mixed, upper_inv)
    return (basis, upper)


def solution(mesh):
    in_specs = (P("shift", "rows", None), P("shift", None))
    out_specs = (P(("rows", "shift"), None), P())
    return jax.shard_map(shards, mesh=mesh, in_specs=in_specs, out_specs=out_specs, check_vma=False)
```

```python
import jax
import jax.numpy as jnp
from jax import lax
from jax.experimental import pallas as pl
from jax.experimental.pallas import tpu as pltpu
from jax.sharding import PartitionSpec as P

HIGHEST = lax.Precision.HIGHEST


def cross_products(left, right):
    return jnp.dot(left.T, right, precision=lax.Precision.HIGH, preferred_element_type=jnp.float32)


def dot_high(a, b):
    return jnp.dot(a, b, precision=lax.Precision.HIGH, preferred_element_type=jnp.float32)


def butterfly_sum(x, axes):
    size = lax.axis_size(axes)
    bit = 1
    while bit < size:
        pairs = [(i, i ^ bit) for i in range(size)]
        x = x + lax.ppermute(x, axes, pairs)
        bit *= 2
    return x


def dot(a, b):
    return jnp.dot(a, b, precision=HIGHEST, preferred_element_type=jnp.float32)


def leaf_factor(a, work):
    del work
    m, width = a.shape
    rows = lax.broadcasted_iota(jnp.int32, (m, width), 0)
    cols = lax.broadcasted_iota(jnp.int32, (m, width), 1)
    current = jnp.where(cols < m, a, (cols - m == rows).astype(jnp.float32))
    row_index = lax.broadcasted_iota(jnp.int32, (m, 1), 0)
    for j in range(m):
        row = current[j:j + 1, :]
        scale = 1.0 / jnp.sqrt(row[:, j:j + 1])
        scaled = row * scale
        coef = jnp.where(row_index > j, current[:, j:j + 1] * scale, 0.0)
        current = jnp.where(row_index == j, scaled, current - coef * scaled)
    upper = jnp.where((cols >= rows) & (cols < m), current, 0.0)
    inverse = jnp.where(cols >= m, current, 0.0)
    return upper, inverse


def factor_half(x, work):
    n = x.shape[0]
    m = n // 2
    cols = lax.broadcasted_iota(jnp.int32, (m, n), 1)
    zeros = jnp.zeros((m, n), jnp.float32)
    r11, l11i_high = leaf_factor(x[:m, :], work)
    l11i = pltpu.roll(l11i_high, m, 1)
    r12 = jnp.where(cols >= m, dot(l11i, x), 0.0)
    r12_full = jnp.concatenate([r12, zeros], axis=0)
    schur_rows = (x - dot(r12_full.T, r12_full))[m:, :]
    r22, l22i_high = leaf_factor(pltpu.roll(schur_rows, m, 1), work)
    upper = jnp.concatenate([r11 + r12, pltpu.roll(r22, m, 1)], axis=0)
    first = jnp.concatenate([l11i, zeros], axis=0)
    second = jnp.concatenate([zeros, l22i_high], axis=0)
    inverse = first + second - dot(dot(second, r12_full.T), first)
    return upper, inverse


def factor_kernel(gram_ref, r_ref, rinv_ref, work):
    n = gram_ref.shape[0]
    h = n // 2
    g = gram_ref[...]
    r11, l11i = factor_half(g[:h, :h], work)
    r12 = dot(l11i, g[:h, h:])
    schur = g[h:, h:] - dot(r12.T, r12)
    r22, l22i = factor_half(schur, work)
    r11i = l11i.T
    r22i = l22i.T
    rinv12 = -dot(dot(r11i, r12), r22i)
    zero = jnp.zeros((h, h), jnp.float32)
    r_ref[:h, :h] = r11
    r_ref[:h, h:] = r12
    r_ref[h:, :h] = zero
    r_ref[h:, h:] = r22
    rinv_ref[:h, :h] = r11i
    rinv_ref[:h, h:] = rinv12
    rinv_ref[h:, :h] = zero
    rinv_ref[h:, h:] = r22i


def factor(gram):
    n = gram.shape[0]
    vmem = pl.BlockSpec(memory_space=pltpu.VMEM)
    return pl.pallas_call(
        factor_kernel,
        out_shape=(jax.ShapeDtypeStruct((n, n), jnp.float32), jax.ShapeDtypeStruct((n, n), jnp.float32)),
        in_specs=[vmem],
        out_specs=(vmem, vmem),
        scratch_shapes=[pltpu.VMEM((n // 4, n // 2), jnp.float32)],
    )(gram)


def shards(filtered, weights):
    weighted = filtered[0].astype(jnp.float32) * weights[0][None, :]
    mixed = lax.psum_scatter(weighted, "shift", scatter_dimension=0, tiled=True)
    devices_all = lax.axis_size(("shift", "rows"))
    total_rows = mixed.shape[0] * devices_all
    gram = cross_products(mixed, mixed) / total_rows
    upper, upper_inv = factor(butterfly_sum(gram, ("shift", "rows")))
    basis = dot_high(mixed, upper_inv)
    return (basis, upper)


def solution(mesh):
    in_specs = (P("shift", "rows", None), P("shift", None))
    out_specs = (P(("rows", "shift"), None), P())
    return jax.shard_map(shards, mesh=mesh, in_specs=in_specs, out_specs=out_specs, check_vma=False)
```

```python
import jax
import jax.numpy as jnp
from jax import lax
from jax.experimental import pallas as pl
from jax.experimental.pallas import tpu as pltpu
from jax.sharding import PartitionSpec as P

HIGHEST = lax.Precision.HIGHEST


def cross_products(left, right):
    return jnp.dot(left.T, right, precision=lax.Precision.HIGH, preferred_element_type=jnp.float32)


def dot_high(a, b):
    return jnp.dot(a, b, precision=lax.Precision.HIGH, preferred_element_type=jnp.float32)


def butterfly_sum(x, axes):
    size = lax.axis_size(axes)
    bit = 1
    while bit < size:
        pairs = [(i, i ^ bit) for i in range(size)]
        x = x + lax.ppermute(x, axes, pairs)
        bit *= 2
    return x


def dot(a, b):
    return jnp.dot(a, b, precision=HIGHEST, preferred_element_type=jnp.float32)


def leaf_factor(a, work):
    del work
    m, width = a.shape
    rows = lax.broadcasted_iota(jnp.int32, (m, width), 0)
    cols = lax.broadcasted_iota(jnp.int32, (m, width), 1)
    current = jnp.where(cols < m, a, (cols - m == rows).astype(jnp.float32))
    row_index = lax.broadcasted_iota(jnp.int32, (m, 1), 0)
    for j in range(m):
        row = current[j:j + 1, :]
        scale = 1.0 / jnp.sqrt(row[:, j:j + 1])
        scaled = row * scale
        coef = jnp.where(row_index > j, current[:, j:j + 1] * scale, 0.0)
        current = jnp.where(row_index == j, scaled, current - coef * scaled)
    upper = jnp.where((cols >= rows) & (cols < m), current, 0.0)
    inverse = jnp.where(cols >= m, current, 0.0)
    return upper, inverse


def factor_half(x, work):
    n = x.shape[0]
    m = n // 2
    cols = lax.broadcasted_iota(jnp.int32, (m, n), 1)
    zeros = jnp.zeros((m, n), jnp.float32)
    r11, l11i_high = leaf_factor(x[:m, :], work)
    l11i = pltpu.roll(l11i_high, m, 1)
    r12 = jnp.where(cols >= m, dot(l11i, x), 0.0)
    r12_full = jnp.concatenate([r12, zeros], axis=0)
    schur_rows = (x - dot(r12_full.T, r12_full))[m:, :]
    r22, l22i_high = leaf_factor(pltpu.roll(schur_rows, m, 1), work)
    upper = jnp.concatenate([r11 + r12, pltpu.roll(r22, m, 1)], axis=0)
    first = jnp.concatenate([l11i, zeros], axis=0)
    second = jnp.concatenate([zeros, l22i_high], axis=0)
    inverse = first + second - dot(dot(second, r12_full.T), first)
    return upper, inverse


def factor_kernel(gram_ref, r_ref, rinv_ref, work):
    h = gram_ref.shape[1]
    g = gram_ref[...]
    r11, l11i = factor_half(g[:h], work)
    r12 = dot(l11i, g[h:2 * h])
    schur = g[2 * h:] - dot(r12.T, r12)
    r22, l22i = factor_half(schur, work)
    r11i = l11i.T
    r22i = l22i.T
    rinv12 = -dot(dot(r11i, r12), r22i)
    zero = jnp.zeros((h, h), jnp.float32)
    r_ref[:h, :h] = r11
    r_ref[:h, h:] = r12
    r_ref[h:, :h] = zero
    r_ref[h:, h:] = r22
    rinv_ref[:h, :h] = r11i
    rinv_ref[:h, h:] = rinv12
    rinv_ref[h:, :h] = zero
    rinv_ref[h:, h:] = r22i


def factor(gram):
    n = 2 * gram.shape[1]
    vmem = pl.BlockSpec(memory_space=pltpu.VMEM)
    return pl.pallas_call(
        factor_kernel,
        out_shape=(jax.ShapeDtypeStruct((n, n), jnp.float32), jax.ShapeDtypeStruct((n, n), jnp.float32)),
        in_specs=[vmem],
        out_specs=(vmem, vmem),
        scratch_shapes=[pltpu.VMEM((n // 4, n // 2), jnp.float32)],
    )(gram)


def shards(filtered, weights):
    weighted = filtered[0].astype(jnp.float32) * weights[0][None, :]
    mixed = lax.psum_scatter(weighted, "shift", scatter_dimension=0, tiled=True)
    devices_all = lax.axis_size(("shift", "rows"))
    total_rows = mixed.shape[0] * devices_all
    half = mixed.shape[1] // 2
    top = cross_products(mixed[:, :half], mixed)
    bottom = cross_products(mixed[:, half:], mixed[:, half:])
    blocks = jnp.concatenate([top[:, :half], top[:, half:], bottom], axis=0) / total_rows
    upper, upper_inv = factor(butterfly_sum(blocks, ("shift", "rows")))
    basis = dot_high(mixed, upper_inv)
    return (basis, upper)


def solution(mesh):
    in_specs = (P("shift", "rows", None), P("shift", None))
    out_specs = (P(("rows", "shift"), None), P())
    return jax.shard_map(shards, mesh=mesh, in_specs=in_specs, out_specs=out_specs, check_vma=False)
```

```python
import jax
import jax.numpy as jnp
from jax import lax
from jax.experimental import pallas as pl
from jax.experimental.pallas import tpu as pltpu
from jax.sharding import PartitionSpec as P

HIGHEST = lax.Precision.HIGHEST


def cross_products(left, right):
    return jnp.dot(left.T, right, precision=lax.Precision.HIGH, preferred_element_type=jnp.float32)


def dot_high(a, b):
    return jnp.dot(a, b, precision=lax.Precision.HIGH, preferred_element_type=jnp.float32)


def butterfly_sum(x, axes):
    size = lax.axis_size(axes)
    bit = 1
    while bit < size:
        pairs = [(i, i ^ bit) for i in range(size)]
        x = x + lax.ppermute(x, axes, pairs)
        bit *= 2
    return x


def dot(a, b):
    return jnp.dot(a, b, precision=HIGHEST, preferred_element_type=jnp.float32)


def leaf_factor(a, work):
    del work
    m, width = a.shape
    rows = lax.broadcasted_iota(jnp.int32, (m, width), 0)
    cols = lax.broadcasted_iota(jnp.int32, (m, width), 1)
    current = jnp.where(cols < m, a, (cols - m == rows).astype(jnp.float32))
    row_index = lax.broadcasted_iota(jnp.int32, (m, 1), 0)
    for j in range(m):
        row = current[j:j + 1, :]
        scale = 1.0 / jnp.sqrt(row[:, j:j + 1])
        scaled = row * scale
        coef = jnp.where(row_index > j, current[:, j:j + 1] * scale, 0.0)
        current = jnp.where(row_index == j, scaled, current - coef * scaled)
    upper = jnp.where((cols >= rows) & (cols < m), current, 0.0)
    inverse = jnp.where(cols >= m, current, 0.0)
    return upper, inverse


def factor_half(x, work):
    n = x.shape[0]
    m = n // 2
    cols = lax.broadcasted_iota(jnp.int32, (m, n), 1)
    zeros = jnp.zeros((m, n), jnp.float32)
    r11, l11i_high = leaf_factor(x[:m, :], work)
    l11i = pltpu.roll(l11i_high, m, 1)
    r12 = jnp.where(cols >= m, dot(l11i, x), 0.0)
    r12_full = jnp.concatenate([r12, zeros], axis=0)
    schur_rows = (x - dot(r12_full.T, r12_full))[m:, :]
    r22, l22i_high = leaf_factor(pltpu.roll(schur_rows, m, 1), work)
    upper = jnp.concatenate([r11 + r12, pltpu.roll(r22, m, 1)], axis=0)
    first = jnp.concatenate([l11i, zeros], axis=0)
    second = jnp.concatenate([zeros, l22i_high], axis=0)
    inverse = first + second - dot(dot(second, r12_full.T), first)
    return upper, inverse


def factor_kernel(gram_ref, r_ref, rinv_ref, work):
    h = gram_ref.shape[1]
    g = gram_ref[...]
    r11, l11i = factor_half(g[:h], work)
    r12 = dot(l11i, g[h:2 * h])
    schur = g[2 * h:] - dot(r12.T, r12)
    r22, l22i = factor_half(schur, work)
    r11i = l11i.T
    r22i = l22i.T
    rinv12 = -dot(dot(r11i, r12), r22i)
    zero = jnp.zeros((h, h), jnp.float32)
    r_ref[:h, :h] = r11
    r_ref[:h, h:] = r12
    r_ref[h:, :h] = zero
    r_ref[h:, h:] = r22
    rinv_ref[:h, :h] = r11i
    rinv_ref[:h, h:] = rinv12
    rinv_ref[h:, :h] = zero
    rinv_ref[h:, h:] = r22i


def factor(gram):
    n = 2 * gram.shape[1]
    vmem = pl.BlockSpec(memory_space=pltpu.VMEM)
    return pl.pallas_call(
        factor_kernel,
        out_shape=(jax.ShapeDtypeStruct((n, n), jnp.float32), jax.ShapeDtypeStruct((n, n), jnp.float32)),
        in_specs=[vmem],
        out_specs=(vmem, vmem),
        scratch_shapes=[pltpu.VMEM((n // 4, n // 2), jnp.float32)],
    )(gram)


def swap(x, bit):
    size = lax.axis_size("shift")
    return lax.ppermute(x, "shift", [(i, i ^ bit) for i in range(size)])


def take(x, index, axis):
    return lax.dynamic_index_in_dim(x, index, axis=axis, keepdims=False)


def mix_rows(filtered, weights):
    shift = lax.axis_index("shift")
    low, high = shift % 2, shift // 2
    rows, width = filtered.shape[1], filtered.shape[2]
    piece = rows // 8
    blocks = filtered[0].reshape(2, 2, 2, piece, width)
    scale = weights[0][None, None, :]

    def weighted(x):
        return x.astype(jnp.float32) * scale

    send_first = weighted(take(blocks[:, :, 0], 1 - low, 1))
    send_second = weighted(take(blocks[:, :, 1], 1 - high, 0))
    send_first, send_second = lax.optimization_barrier((send_first, send_second))
    got_first, got_second = swap(send_first, 1), swap(send_second, 2)
    first = weighted(take(blocks[:, :, 0], low, 1)) + got_first
    second = weighted(take(blocks[:, :, 1], high, 0)) + got_second
    send_first, send_second = take(first, 1 - high, 0), take(second, 1 - low, 0)
    send_first, send_second = lax.optimization_barrier((send_first, send_second))
    got_first, got_second = swap(send_first, 2), swap(send_second, 1)
    first = take(first, high, 0) + got_first
    second = take(second, low, 0) + got_second
    return jnp.concatenate([first, second], axis=0)


def shards(filtered, weights):
    if lax.axis_size("shift") == 4:
        mixed = mix_rows(filtered, weights)
    else:
        weighted = filtered[0].astype(jnp.float32) * weights[0][None, :]
        mixed = lax.psum_scatter(weighted, "shift", scatter_dimension=0, tiled=True)
    devices_all = lax.axis_size(("shift", "rows"))
    total_rows = mixed.shape[0] * devices_all
    half = mixed.shape[1] // 2
    top = cross_products(mixed[:, :half], mixed)
    bottom = cross_products(mixed[:, half:], mixed[:, half:])
    blocks = jnp.concatenate([top[:, :half], top[:, half:], bottom], axis=0) / total_rows
    upper, upper_inv = factor(butterfly_sum(blocks, ("shift", "rows")))
    basis = dot_high(mixed, upper_inv)
    return (basis, upper)


def solution(mesh):
    in_specs = (P("shift", "rows", None), P("shift", None))
    out_specs = (P(("rows", "shift"), None), P())
    return jax.shard_map(shards, mesh=mesh, in_specs=in_specs, out_specs=out_specs, check_vma=False)
```

```python
import jax
import jax.numpy as jnp
from jax import lax
from jax.experimental import pallas as pl
from jax.experimental.pallas import tpu as pltpu
from jax.sharding import PartitionSpec as P

HIGHEST = lax.Precision.HIGHEST


def cross_products(left, right):
    return jnp.dot(left.T, right, precision=lax.Precision.HIGH, preferred_element_type=jnp.float32)


def dot_high(a, b):
    return jnp.dot(a, b, precision=lax.Precision.HIGH, preferred_element_type=jnp.float32)


def butterfly_sum(x, axes):
    size = lax.axis_size(axes)
    bit = 1
    while bit < size:
        pairs = [(i, i ^ bit) for i in range(size)]
        x = x + lax.ppermute(x, axes, pairs)
        bit *= 2
    return x


def dot(a, b):
    return jnp.dot(a, b, precision=HIGHEST, preferred_element_type=jnp.float32)


def leaf_factor(a, work):
    del work
    m, width = a.shape
    rows = lax.broadcasted_iota(jnp.int32, (m, width), 0)
    cols = lax.broadcasted_iota(jnp.int32, (m, width), 1)
    current = jnp.where(cols < m, a, (cols - m == rows).astype(jnp.float32))
    row_index = lax.broadcasted_iota(jnp.int32, (m, 1), 0)
    for j in range(m):
        row = current[j:j + 1, :]
        scale = 1.0 / jnp.sqrt(row[:, j:j + 1])
        scaled = row * scale
        coef = jnp.where(row_index > j, current[:, j:j + 1] * scale, 0.0)
        current = jnp.where(row_index == j, scaled, current - coef * scaled)
    upper = jnp.where((cols >= rows) & (cols < m), current, 0.0)
    inverse = jnp.where(cols >= m, current, 0.0)
    return upper, inverse


def factor_half(x, work):
    n = x.shape[0]
    m = n // 2
    cols = lax.broadcasted_iota(jnp.int32, (m, n), 1)
    zeros = jnp.zeros((m, n), jnp.float32)
    r11, l11i_high = leaf_factor(x[:m, :], work)
    l11i = pltpu.roll(l11i_high, m, 1)
    r12 = jnp.where(cols >= m, dot(l11i, x), 0.0)
    r12_full = jnp.concatenate([r12, zeros], axis=0)
    schur_rows = (x - dot(r12_full.T, r12_full))[m:, :]
    r22, l22i_high = leaf_factor(pltpu.roll(schur_rows, m, 1), work)
    upper = jnp.concatenate([r11 + r12, pltpu.roll(r22, m, 1)], axis=0)
    first = jnp.concatenate([l11i, zeros], axis=0)
    second = jnp.concatenate([zeros, l22i_high], axis=0)
    inverse = first + second - dot(dot(second, r12_full.T), first)
    return upper, inverse


def factor_kernel(gram_ref, r_ref, rinv_ref, work):
    h = gram_ref.shape[1]
    g = gram_ref[...]
    r11, l11i = factor_half(g[:h], work)
    r12 = dot(l11i, g[h:2 * h])
    schur = g[2 * h:] - dot(r12.T, r12)
    r22, l22i = factor_half(schur, work)
    r11i = l11i.T
    r22i = l22i.T
    rinv12 = -dot(dot(r11i, r12), r22i)
    zero = jnp.zeros((h, h), jnp.float32)
    r_ref[:h, :h] = r11
    r_ref[:h, h:] = r12
    r_ref[h:, :h] = zero
    r_ref[h:, h:] = r22
    rinv_ref[:h, :h] = r11i
    rinv_ref[:h, h:] = rinv12
    rinv_ref[h:, :h] = zero
    rinv_ref[h:, h:] = r22i


def factor(gram):
    n = 2 * gram.shape[1]
    vmem = pl.BlockSpec(memory_space=pltpu.VMEM)
    return pl.pallas_call(
        factor_kernel,
        out_shape=(jax.ShapeDtypeStruct((n, n), jnp.float32), jax.ShapeDtypeStruct((n, n), jnp.float32)),
        in_specs=[vmem],
        out_specs=(vmem, vmem),
        scratch_shapes=[pltpu.VMEM((n // 4, n // 2), jnp.float32)],
    )(gram)


def swap(x, bit):
    size = lax.axis_size("shift")
    return lax.ppermute(x, "shift", [(i, i ^ bit) for i in range(size)])


def take(x, index, axis):
    return lax.dynamic_index_in_dim(x, index, axis=axis, keepdims=False)


def mix_rows(filtered, weights):
    shift = lax.axis_index("shift")
    low, high = shift % 2, shift // 2
    rows, width = filtered.shape[1], filtered.shape[2]
    block, piece = rows // 4, rows // 8
    scale = weights[0][None, :]

    def part(chunk, half):
        start = chunk * block + half * piece
        values = lax.dynamic_slice_in_dim(filtered[0], start, piece, axis=0)
        return values.astype(jnp.float32) * scale

    sends = [part(2 * hi + 1 - low, 0) for hi in range(2)] + [part(2 * (1 - high) + lo, 1) for lo in range(2)]
    sends = lax.optimization_barrier(sends)
    got = [swap(sends[0], 1), swap(sends[1], 1), swap(sends[2], 2), swap(sends[3], 2)]
    first = [part(2 * hi + low, 0) + got[hi] for hi in range(2)]
    second = [part(2 * high + lo, 1) + got[2 + lo] for lo in range(2)]
    send_first = jnp.where(high == 0, first[1], first[0])
    send_second = jnp.where(low == 0, second[1], second[0])
    send_first, send_second = lax.optimization_barrier((send_first, send_second))
    got_first, got_second = swap(send_first, 2), swap(send_second, 1)
    first = jnp.where(high == 0, first[0], first[1]) + got_first
    second = jnp.where(low == 0, second[0], second[1]) + got_second
    return jnp.concatenate([first, second], axis=0)


def shards(filtered, weights):
    if lax.axis_size("shift") == 4:
        mixed = mix_rows(filtered, weights)
    else:
        weighted = filtered[0].astype(jnp.float32) * weights[0][None, :]
        mixed = lax.psum_scatter(weighted, "shift", scatter_dimension=0, tiled=True)
    devices_all = lax.axis_size(("shift", "rows"))
    total_rows = mixed.shape[0] * devices_all
    half = mixed.shape[1] // 2
    top = cross_products(mixed[:, :half], mixed)
    bottom = cross_products(mixed[:, half:], mixed[:, half:])
    blocks = jnp.concatenate([top[:, :half], top[:, half:], bottom], axis=0) / total_rows
    upper, upper_inv = factor(butterfly_sum(blocks, ("shift", "rows")))
    basis = dot_high(mixed, upper_inv)
    return (basis, upper)


def solution(mesh):
    in_specs = (P("shift", "rows", None), P("shift", None))
    out_specs = (P(("rows", "shift"), None), P())
    return jax.shard_map(shards, mesh=mesh, in_specs=in_specs, out_specs=out_specs, check_vma=False)
```

```python
import jax
import jax.numpy as jnp
from jax import lax
from jax.experimental import pallas as pl
from jax.experimental.pallas import tpu as pltpu
from jax.sharding import PartitionSpec as P

HIGHEST = lax.Precision.HIGHEST


def cross_products(left, right):
    return jnp.dot(left.T, right, precision=lax.Precision.HIGH, preferred_element_type=jnp.float32)


def dot_high(a, b):
    return jnp.dot(a, b, precision=lax.Precision.HIGH, preferred_element_type=jnp.float32)


def butterfly_sum(x, axes):
    size = lax.axis_size(axes)
    bit = 1
    while bit < size:
        pairs = [(i, i ^ bit) for i in range(size)]
        x = x + lax.ppermute(x, axes, pairs)
        bit *= 2
    return x


def dot(a, b):
    return jnp.dot(a, b, precision=HIGHEST, preferred_element_type=jnp.float32)


def leaf_factor(a, work):
    del work
    m, width = a.shape
    rows = lax.broadcasted_iota(jnp.int32, (m, width), 0)
    cols = lax.broadcasted_iota(jnp.int32, (m, width), 1)
    current = jnp.where(cols < m, a, (cols - m == rows).astype(jnp.float32))
    row_index = lax.broadcasted_iota(jnp.int32, (m, 1), 0)
    for j in range(m):
        row = current[j:j + 1, :]
        scale = 1.0 / jnp.sqrt(row[:, j:j + 1])
        scaled = row * scale
        coef = jnp.where(row_index > j, current[:, j:j + 1] * scale, 0.0)
        current = jnp.where(row_index == j, scaled, current - coef * scaled)
    upper = jnp.where((cols >= rows) & (cols < m), current, 0.0)
    inverse = jnp.where(cols >= m, current, 0.0)
    return upper, inverse


def factor_half(x, work):
    n = x.shape[0]
    m = n // 2
    cols = lax.broadcasted_iota(jnp.int32, (m, n), 1)
    zeros = jnp.zeros((m, n), jnp.float32)
    r11, l11i_high = leaf_factor(x[:m, :], work)
    l11i = pltpu.roll(l11i_high, m, 1)
    r12 = jnp.where(cols >= m, dot(l11i, x), 0.0)
    r12_full = jnp.concatenate([r12, zeros], axis=0)
    schur_rows = (x - dot(r12_full.T, r12_full))[m:, :]
    r22, l22i_high = leaf_factor(pltpu.roll(schur_rows, m, 1), work)
    upper = jnp.concatenate([r11 + r12, pltpu.roll(r22, m, 1)], axis=0)
    first = jnp.concatenate([l11i, zeros], axis=0)
    second = jnp.concatenate([zeros, l22i_high], axis=0)
    inverse = first + second - dot(dot(second, r12_full.T), first)
    return upper, inverse


def factor_kernel(gram_ref, r_ref, rinv_ref, work):
    h = gram_ref.shape[1]
    g = gram_ref[...]
    r11, l11i = factor_half(g[:h], work)
    r12 = dot(l11i, g[h:2 * h])
    schur = g[2 * h:] - dot(r12.T, r12)
    r22, l22i = factor_half(schur, work)
    r11i = l11i.T
    r22i = l22i.T
    rinv12 = -dot(dot(r11i, r12), r22i)
    zero = jnp.zeros((h, h), jnp.float32)
    r_ref[:h, :h] = r11
    r_ref[:h, h:] = r12
    r_ref[h:, :h] = zero
    r_ref[h:, h:] = r22
    rinv_ref[:h, :h] = r11i
    rinv_ref[:h, h:] = rinv12
    rinv_ref[h:, :h] = zero
    rinv_ref[h:, h:] = r22i


def factor(gram):
    n = 2 * gram.shape[1]
    vmem = pl.BlockSpec(memory_space=pltpu.VMEM)
    return pl.pallas_call(
        factor_kernel,
        out_shape=(jax.ShapeDtypeStruct((n, n), jnp.float32), jax.ShapeDtypeStruct((n, n), jnp.float32)),
        in_specs=[vmem],
        out_specs=(vmem, vmem),
        scratch_shapes=[pltpu.VMEM((n // 4, n // 2), jnp.float32)],
    )(gram)


def swap(x, bit):
    size = lax.axis_size("shift")
    return lax.ppermute(x, "shift", [(i, i ^ bit) for i in range(size)])


def take(x, index, axis):
    return lax.dynamic_index_in_dim(x, index, axis=axis, keepdims=False)


def mix_rows(filtered, weights):
    shift = lax.axis_index("shift")
    low, high = shift % 2, shift // 2
    rows, width = filtered.shape[1], filtered.shape[2]
    block, piece = rows // 4, rows // 8
    scale = weights[0][None, :]

    def part(chunk, half):
        start = chunk * block + half * piece
        values = lax.dynamic_slice_in_dim(filtered[0], start, piece, axis=0)
        return values.astype(jnp.float32) * scale

    forward_x = part(2 * (1 - high) + 1 - low, 0)
    forward_y = part(2 * (1 - high) + 1 - low, 1)
    forward_x, forward_y = lax.optimization_barrier((forward_x, forward_y))
    got_forward_x, got_forward_y = swap(forward_x, 1), swap(forward_y, 2)
    stay_x = part(2 * high + 1 - low, 0)
    stay_y = part(2 * (1 - high) + low, 1)
    stay_x, stay_y = lax.optimization_barrier((stay_x, stay_y))
    got_stay_x, got_stay_y = swap(stay_x, 1), swap(stay_y, 2)
    send_first = part(2 * (1 - high) + low, 0) + got_forward_x
    send_second = part(2 * high + 1 - low, 1) + got_forward_y
    send_first, send_second = lax.optimization_barrier((send_first, send_second))
    got_first, got_second = swap(send_first, 2), swap(send_second, 1)
    first = part(2 * high + low, 0) + got_stay_x + got_first
    second = part(2 * high + low, 1) + got_stay_y + got_second
    return jnp.concatenate([first, second], axis=0)


def shards(filtered, weights):
    if lax.axis_size("shift") == 4:
        mixed = mix_rows(filtered, weights)
    else:
        weighted = filtered[0].astype(jnp.float32) * weights[0][None, :]
        mixed = lax.psum_scatter(weighted, "shift", scatter_dimension=0, tiled=True)
    devices_all = lax.axis_size(("shift", "rows"))
    total_rows = mixed.shape[0] * devices_all
    half = mixed.shape[1] // 2
    top = cross_products(mixed[:, :half], mixed)
    bottom = cross_products(mixed[:, half:], mixed[:, half:])
    blocks = jnp.concatenate([top[:, :half], top[:, half:], bottom], axis=0) / total_rows
    upper, upper_inv = factor(butterfly_sum(blocks, ("shift", "rows")))
    basis = dot_high(mixed, upper_inv)
    return (basis, upper)


def solution(mesh):
    in_specs = (P("shift", "rows", None), P("shift", None))
    out_specs = (P(("rows", "shift"), None), P())
    return jax.shard_map(shards, mesh=mesh, in_specs=in_specs, out_specs=out_specs, check_vma=False)
```

```python
import jax
import jax.numpy as jnp
from jax import lax
from jax.experimental import pallas as pl
from jax.experimental.pallas import tpu as pltpu
from jax.sharding import PartitionSpec as P

HIGHEST = lax.Precision.HIGHEST


def cross_products(left, right):
    return jnp.dot(left.T, right, precision=lax.Precision.HIGH, preferred_element_type=jnp.float32)


def dot_high(a, b):
    return jnp.dot(a, b, precision=lax.Precision.HIGH, preferred_element_type=jnp.float32)


def butterfly_sum(x, axes):
    size = lax.axis_size(axes)

    def exchange(value, mask):
        pairs = [(i, i ^ mask) for i in range(size)]
        return lax.ppermute(value, axes, pairs)

    bits = []
    bit = 1
    while bit < size:
        bits.append(bit)
        bit *= 2
    groups = [bits[:1]] + [bits[i:i + 2] for i in range(1, len(bits), 2)]
    for group in groups:
        if len(group) == 1:
            x = x + exchange(x, group[0])
        else:
            near, far = group
            own_pair = x + exchange(x, near)
            other_pair = exchange(x, far) + exchange(x, near | far)
            x = own_pair + other_pair
    return x


def dot(a, b):
    return jnp.dot(a, b, precision=HIGHEST, preferred_element_type=jnp.float32)


def leaf_factor(a, work):
    del work
    m, width = a.shape
    rows = lax.broadcasted_iota(jnp.int32, (m, width), 0)
    cols = lax.broadcasted_iota(jnp.int32, (m, width), 1)
    current = jnp.where(cols < m, a, (cols - m == rows).astype(jnp.float32))
    row_index = lax.broadcasted_iota(jnp.int32, (m, 1), 0)
    for j in range(m):
        row = current[j:j + 1, :]
        scale = 1.0 / jnp.sqrt(row[:, j:j + 1])
        scaled = row * scale
        coef = jnp.where(row_index > j, current[:, j:j + 1] * scale, 0.0)
        current = jnp.where(row_index == j, scaled, current - coef * scaled)
    upper = jnp.where((cols >= rows) & (cols < m), current, 0.0)
    inverse = jnp.where(cols >= m, current, 0.0)
    return upper, inverse


def factor_half(x, work):
    n = x.shape[0]
    m = n // 2
    cols = lax.broadcasted_iota(jnp.int32, (m, n), 1)
    zeros = jnp.zeros((m, n), jnp.float32)
    r11, l11i_high = leaf_factor(x[:m, :], work)
    l11i = pltpu.roll(l11i_high, m, 1)
    r12 = jnp.where(cols >= m, dot(l11i, x), 0.0)
    r12_full = jnp.concatenate([r12, zeros], axis=0)
    schur_rows = (x - dot(r12_full.T, r12_full))[m:, :]
    r22, l22i_high = leaf_factor(pltpu.roll(schur_rows, m, 1), work)
    upper = jnp.concatenate([r11 + r12, pltpu.roll(r22, m, 1)], axis=0)
    first = jnp.concatenate([l11i, zeros], axis=0)
    second = jnp.concatenate([zeros, l22i_high], axis=0)
    inverse = first + second - dot(dot(second, r12_full.T), first)
    return upper, inverse


def factor_kernel(gram_ref, r_ref, rinv_ref, work):
    h = gram_ref.shape[1]
    g = gram_ref[...]
    r11, l11i = factor_half(g[:h], work)
    r12 = dot(l11i, g[h:2 * h])
    schur = g[2 * h:] - dot(r12.T, r12)
    r22, l22i = factor_half(schur, work)
    r11i = l11i.T
    r22i = l22i.T
    rinv12 = -dot(dot(r11i, r12), r22i)
    zero = jnp.zeros((h, h), jnp.float32)
    r_ref[:h, :h] = r11
    r_ref[:h, h:] = r12
    r_ref[h:, :h] = zero
    r_ref[h:, h:] = r22
    rinv_ref[:h, :h] = r11i
    rinv_ref[:h, h:] = rinv12
    rinv_ref[h:, :h] = zero
    rinv_ref[h:, h:] = r22i


def factor(gram):
    n = 2 * gram.shape[1]
    vmem = pl.BlockSpec(memory_space=pltpu.VMEM)
    return pl.pallas_call(
        factor_kernel,
        out_shape=(jax.ShapeDtypeStruct((n, n), jnp.float32), jax.ShapeDtypeStruct((n, n), jnp.float32)),
        in_specs=[vmem],
        out_specs=(vmem, vmem),
        scratch_shapes=[pltpu.VMEM((n // 4, n // 2), jnp.float32)],
    )(gram)


def swap(x, bit):
    size = lax.axis_size("shift")
    return lax.ppermute(x, "shift", [(i, i ^ bit) for i in range(size)])


def take(x, index, axis):
    return lax.dynamic_index_in_dim(x, index, axis=axis, keepdims=False)


def mix_rows(filtered, weights):
    shift = lax.axis_index("shift")
    low, high = shift % 2, shift // 2
    rows, width = filtered.shape[1], filtered.shape[2]
    block, piece = rows // 4, rows // 8
    scale = weights[0][None, :]

    def part(chunk, half):
        start = chunk * block + half * piece
        values = lax.dynamic_slice_in_dim(filtered[0], start, piece, axis=0)
        return values.astype(jnp.float32) * scale

    forward_x = part(2 * (1 - high) + 1 - low, 0)
    forward_y = part(2 * (1 - high) + 1 - low, 1)
    forward_x, forward_y = lax.optimization_barrier((forward_x, forward_y))
    got_forward_x, got_forward_y = swap(forward_x, 1), swap(forward_y, 2)
    stay_x = part(2 * high + 1 - low, 0)
    stay_y = part(2 * (1 - high) + low, 1)
    stay_x, stay_y = lax.optimization_barrier((stay_x, stay_y))
    got_stay_x, got_stay_y = swap(stay_x, 1), swap(stay_y, 2)
    send_first = part(2 * (1 - high) + low, 0) + got_forward_x
    send_second = part(2 * high + 1 - low, 1) + got_forward_y
    send_first, send_second = lax.optimization_barrier((send_first, send_second))
    got_first, got_second = swap(send_first, 2), swap(send_second, 1)
    first = part(2 * high + low, 0) + got_stay_x + got_first
    second = part(2 * high + low, 1) + got_stay_y + got_second
    return jnp.concatenate([first, second], axis=0)


def shards(filtered, weights):
    if lax.axis_size("shift") == 4:
        mixed = mix_rows(filtered, weights)
    else:
        weighted = filtered[0].astype(jnp.float32) * weights[0][None, :]
        mixed = lax.psum_scatter(weighted, "shift", scatter_dimension=0, tiled=True)
    devices_all = lax.axis_size(("shift", "rows"))
    total_rows = mixed.shape[0] * devices_all
    half = mixed.shape[1] // 2
    top = cross_products(mixed[:, :half], mixed)
    bottom = cross_products(mixed[:, half:], mixed[:, half:])
    blocks = jnp.concatenate([top[:, :half], top[:, half:], bottom], axis=0) / total_rows
    upper, upper_inv = factor(butterfly_sum(blocks, ("shift", "rows")))
    basis = dot_high(mixed, upper_inv)
    return (basis, upper)


def solution(mesh):
    in_specs = (P("shift", "rows", None), P("shift", None))
    out_specs = (P(("rows", "shift"), None), P())
    return jax.shard_map(shards, mesh=mesh, in_specs=in_specs, out_specs=out_specs, check_vma=False)
```

```python
import jax
import jax.numpy as jnp
from jax import lax
from jax.experimental import pallas as pl
from jax.experimental.pallas import tpu as pltpu
from jax.sharding import PartitionSpec as P

HIGHEST = lax.Precision.HIGHEST


def cross_products(left, right):
    return jnp.dot(left.T, right, precision=lax.Precision.HIGH, preferred_element_type=jnp.float32)


def dot_high(a, b):
    return jnp.dot(a, b, precision=lax.Precision.HIGH, preferred_element_type=jnp.float32)


def butterfly_sum(x, axes):
    size = lax.axis_size(axes)
    bit = 1
    while bit < size:
        pairs = [(i, i ^ bit) for i in range(size)]
        x = x + lax.ppermute(x, axes, pairs)
        bit *= 2
    return x


def dot(a, b):
    return jnp.dot(a, b, precision=HIGHEST, preferred_element_type=jnp.float32)


def leaf_factor(a, work):
    del work
    m, width = a.shape
    rows = lax.broadcasted_iota(jnp.int32, (m, width), 0)
    cols = lax.broadcasted_iota(jnp.int32, (m, width), 1)
    current = jnp.where(cols < m, a, (cols - m == rows).astype(jnp.float32))
    row_index = lax.broadcasted_iota(jnp.int32, (m, 1), 0)
    for j in range(m):
        row = current[j:j + 1, :]
        scale = 1.0 / jnp.sqrt(row[:, j:j + 1])
        scaled = row * scale
        coef = jnp.where(row_index > j, current[:, j:j + 1] * scale, 0.0)
        current = jnp.where(row_index == j, scaled, current - coef * scaled)
    upper = jnp.where((cols >= rows) & (cols < m), current, 0.0)
    inverse = jnp.where(cols >= m, current, 0.0)
    return upper, inverse


def factor_half(x, work):
    n = x.shape[0]
    m = n // 2
    cols = lax.broadcasted_iota(jnp.int32, (m, n), 1)
    zeros = jnp.zeros((m, n), jnp.float32)
    r11, l11i_high = leaf_factor(x[:m, :], work)
    l11i = pltpu.roll(l11i_high, m, 1)
    r12 = jnp.where(cols >= m, dot(l11i, x), 0.0)
    r12_full = jnp.concatenate([r12, zeros], axis=0)
    schur_rows = (x - dot(r12_full.T, r12_full))[m:, :]
    r22, l22i_high = leaf_factor(pltpu.roll(schur_rows, m, 1), work)
    upper = jnp.concatenate([r11 + r12, pltpu.roll(r22, m, 1)], axis=0)
    first = jnp.concatenate([l11i, zeros], axis=0)
    second = jnp.concatenate([zeros, l22i_high], axis=0)
    inverse = first + second - dot(dot(second, r12_full.T), first)
    return upper, inverse


def factor_kernel(gram_ref, r_ref, rinv_ref, work):
    h = gram_ref.shape[1]
    g = gram_ref[...]
    r11, l11i = factor_half(g[:h], work)
    r12 = dot(l11i, g[h:2 * h])
    schur = g[2 * h:] - dot(r12.T, r12)
    r22, l22i = factor_half(schur, work)
    r11i = l11i.T
    r22i = l22i.T
    rinv12 = -dot(dot(r11i, r12), r22i)
    zero = jnp.zeros((h, h), jnp.float32)
    r_ref[:h, :h] = r11
    r_ref[:h, h:] = r12
    r_ref[h:, :h] = zero
    r_ref[h:, h:] = r22
    rinv_ref[:h, :h] = r11i
    rinv_ref[:h, h:] = rinv12
    rinv_ref[h:, :h] = zero
    rinv_ref[h:, h:] = r22i


def factor(gram):
    n = 2 * gram.shape[1]
    vmem = pl.BlockSpec(memory_space=pltpu.VMEM)
    return pl.pallas_call(
        factor_kernel,
        out_shape=(jax.ShapeDtypeStruct((n, n), jnp.float32), jax.ShapeDtypeStruct((n, n), jnp.float32)),
        in_specs=[vmem],
        out_specs=(vmem, vmem),
        scratch_shapes=[pltpu.VMEM((n // 4, n // 2), jnp.float32)],
    )(gram)


def swap(x, bit):
    size = lax.axis_size("shift")
    return lax.ppermute(x, "shift", [(i, i ^ bit) for i in range(size)])


def take(x, index, axis):
    return lax.dynamic_index_in_dim(x, index, axis=axis, keepdims=False)


def mix_rows(filtered, weights):
    shift = lax.axis_index("shift")
    low, high = shift % 2, shift // 2
    rows, width = filtered.shape[1], filtered.shape[2]
    block, piece = rows // 4, rows // 8
    scale = weights[0][None, :]

    def part(chunk, half):
        start = chunk * block + half * piece
        values = lax.dynamic_slice_in_dim(filtered[0], start, piece, axis=0)
        return values.astype(jnp.float32) * scale

    forward_x = part(2 * (1 - high) + 1 - low, 0)
    forward_y = part(2 * (1 - high) + 1 - low, 1)
    forward_x, forward_y = lax.optimization_barrier((forward_x, forward_y))
    got_forward_x, got_forward_y = swap(forward_x, 1), swap(forward_y, 2)
    stay_x = part(2 * high + 1 - low, 0)
    stay_y = part(2 * (1 - high) + low, 1)
    stay_x, stay_y = lax.optimization_barrier((stay_x, stay_y))
    got_stay_x, got_stay_y = swap(stay_x, 1), swap(stay_y, 2)
    send_first = part(2 * (1 - high) + low, 0) + got_forward_x
    send_second = part(2 * high + 1 - low, 1) + got_forward_y
    quarter = piece // 2
    send_first, send_second = lax.optimization_barrier((send_first, send_second))
    got_pieces = []
    for k in range(2):
        rows_k = slice(k * quarter, (k + 1) * quarter)
        got_pieces.append((swap(send_first[rows_k], 2), swap(send_second[rows_k], 1)))
    own_first, own_second = part(2 * high + low, 0), part(2 * high + low, 1)
    pieces = []
    for k in range(2):
        rows_k = slice(k * quarter, (k + 1) * quarter)
        pieces.append((own_first[rows_k] + got_stay_x[rows_k] + got_pieces[k][0],
                       own_second[rows_k] + got_stay_y[rows_k] + got_pieces[k][1]))
    return [pieces[0][0], pieces[1][0], pieces[0][1], pieces[1][1]]


def shards(filtered, weights):
    if lax.axis_size("shift") == 4:
        row_pieces = mix_rows(filtered, weights)
    else:
        weighted = filtered[0].astype(jnp.float32) * weights[0][None, :]
        row_pieces = [lax.psum_scatter(weighted, "shift", scatter_dimension=0, tiled=True)]
    mixed = jnp.concatenate(row_pieces, axis=0)
    devices_all = lax.axis_size(("shift", "rows"))
    total_rows = mixed.shape[0] * devices_all
    half = mixed.shape[1] // 2
    blocks = None
    for rows_k in row_pieces:
        top = cross_products(rows_k[:, :half], rows_k)
        bottom = cross_products(rows_k[:, half:], rows_k[:, half:])
        part_blocks = jnp.concatenate([top[:, :half], top[:, half:], bottom], axis=0)
        blocks = part_blocks if blocks is None else blocks + part_blocks
    blocks = blocks / total_rows
    upper, upper_inv = factor(butterfly_sum(blocks, ("shift", "rows")))
    basis = dot_high(mixed, upper_inv)
    return (basis, upper)


def solution(mesh):
    in_specs = (P("shift", "rows", None), P("shift", None))
    out_specs = (P(("rows", "shift"), None), P())
    return jax.shard_map(shards, mesh=mesh, in_specs=in_specs, out_specs=out_specs, check_vma=False)
```

```python
import jax
import jax.numpy as jnp
from jax import lax
from jax.experimental import pallas as pl
from jax.experimental.pallas import tpu as pltpu
from jax.sharding import PartitionSpec as P

HIGHEST = lax.Precision.HIGHEST


def cross_products(left, right):
    return jnp.dot(left.T, right, precision=lax.Precision.DEFAULT, preferred_element_type=jnp.float32)


def dot_high(a, b):
    return jnp.dot(a, b, precision=lax.Precision.HIGH, preferred_element_type=jnp.float32)


def butterfly_sum(x, axes):
    size = lax.axis_size(axes)
    bit = 1
    while bit < size:
        pairs = [(i, i ^ bit) for i in range(size)]
        x = x + lax.ppermute(x, axes, pairs)
        bit *= 2
    return x


def dot(a, b):
    return jnp.dot(a, b, precision=HIGHEST, preferred_element_type=jnp.float32)


def leaf_factor(a, work):
    del work
    m, width = a.shape
    rows = lax.broadcasted_iota(jnp.int32, (m, width), 0)
    cols = lax.broadcasted_iota(jnp.int32, (m, width), 1)
    current = jnp.where(cols < m, a, (cols - m == rows).astype(jnp.float32))
    row_index = lax.broadcasted_iota(jnp.int32, (m, 1), 0)
    for j in range(m):
        row = current[j:j + 1, :]
        scale = 1.0 / jnp.sqrt(row[:, j:j + 1])
        scaled = row * scale
        coef = jnp.where(row_index > j, current[:, j:j + 1] * scale, 0.0)
        current = jnp.where(row_index == j, scaled, current - coef * scaled)
    upper = jnp.where((cols >= rows) & (cols < m), current, 0.0)
    inverse = jnp.where(cols >= m, current, 0.0)
    return upper, inverse


def factor_half(x, work):
    n = x.shape[0]
    m = n // 2
    cols = lax.broadcasted_iota(jnp.int32, (m, n), 1)
    zeros = jnp.zeros((m, n), jnp.float32)
    r11, l11i_high = leaf_factor(x[:m, :], work)
    l11i = pltpu.roll(l11i_high, m, 1)
    r12 = jnp.where(cols >= m, dot(l11i, x), 0.0)
    r12_full = jnp.concatenate([r12, zeros], axis=0)
    schur_rows = (x - dot(r12_full.T, r12_full))[m:, :]
    r22, l22i_high = leaf_factor(pltpu.roll(schur_rows, m, 1), work)
    upper = jnp.concatenate([r11 + r12, pltpu.roll(r22, m, 1)], axis=0)
    first = jnp.concatenate([l11i, zeros], axis=0)
    second = jnp.concatenate([zeros, l22i_high], axis=0)
    inverse = first + second - dot(dot(second, r12_full.T), first)
    return upper, inverse


def factor_kernel(gram_ref, r_ref, rinv_ref, work):
    h = gram_ref.shape[1]
    g = gram_ref[...]
    r11, l11i = factor_half(g[:h], work)
    r12 = dot(l11i, g[h:2 * h])
    schur = g[2 * h:] - dot(r12.T, r12)
    r22, l22i = factor_half(schur, work)
    r11i = l11i.T
    r22i = l22i.T
    rinv12 = -dot(dot(r11i, r12), r22i)
    zero = jnp.zeros((h, h), jnp.float32)
    r_ref[:h, :h] = r11
    r_ref[:h, h:] = r12
    r_ref[h:, :h] = zero
    r_ref[h:, h:] = r22
    rinv_ref[:h, :h] = r11i
    rinv_ref[:h, h:] = rinv12
    rinv_ref[h:, :h] = zero
    rinv_ref[h:, h:] = r22i


def factor(gram):
    n = 2 * gram.shape[1]
    vmem = pl.BlockSpec(memory_space=pltpu.VMEM)
    return pl.pallas_call(
        factor_kernel,
        out_shape=(jax.ShapeDtypeStruct((n, n), jnp.float32), jax.ShapeDtypeStruct((n, n), jnp.float32)),
        in_specs=[vmem],
        out_specs=(vmem, vmem),
        scratch_shapes=[pltpu.VMEM((n // 4, n // 2), jnp.float32)],
    )(gram)


def swap(x, bit):
    size = lax.axis_size("shift")
    return lax.ppermute(x, "shift", [(i, i ^ bit) for i in range(size)])


def take(x, index, axis):
    return lax.dynamic_index_in_dim(x, index, axis=axis, keepdims=False)


def mix_rows(filtered, weights):
    shift = lax.axis_index("shift")
    low, high = shift % 2, shift // 2
    rows, width = filtered.shape[1], filtered.shape[2]
    block, piece = rows // 4, rows // 8
    scale = weights[0][None, :]

    def part(chunk, half):
        start = chunk * block + half * piece
        values = lax.dynamic_slice_in_dim(filtered[0], start, piece, axis=0)
        return values.astype(jnp.float32) * scale

    forward_x = part(2 * (1 - high) + 1 - low, 0)
    forward_y = part(2 * (1 - high) + 1 - low, 1)
    forward_x, forward_y = lax.optimization_barrier((forward_x, forward_y))
    got_forward_x, got_forward_y = swap(forward_x, 1), swap(forward_y, 2)
    stay_x = part(2 * high + 1 - low, 0)
    stay_y = part(2 * (1 - high) + low, 1)
    stay_x, stay_y = lax.optimization_barrier((stay_x, stay_y))
    got_stay_x, got_stay_y = swap(stay_x, 1), swap(stay_y, 2)
    send_first = part(2 * (1 - high) + low, 0) + got_forward_x
    send_second = part(2 * high + 1 - low, 1) + got_forward_y
    send_first, send_second = lax.optimization_barrier((send_first, send_second))
    got_first, got_second = swap(send_first, 2), swap(send_second, 1)
    first = part(2 * high + low, 0) + got_stay_x + got_first
    second = part(2 * high + low, 1) + got_stay_y + got_second
    return jnp.concatenate([first, second], axis=0)


def shards(filtered, weights):
    if lax.axis_size("shift") == 4:
        mixed = mix_rows(filtered, weights)
    else:
        weighted = filtered[0].astype(jnp.float32) * weights[0][None, :]
        mixed = lax.psum_scatter(weighted, "shift", scatter_dimension=0, tiled=True)
    devices_all = lax.axis_size(("shift", "rows"))
    total_rows = mixed.shape[0] * devices_all
    half = mixed.shape[1] // 2
    top = cross_products(mixed[:, :half], mixed)
    bottom = cross_products(mixed[:, half:], mixed[:, half:])
    blocks = jnp.concatenate([top[:, :half], top[:, half:], bottom], axis=0) / total_rows
    upper, upper_inv = factor(butterfly_sum(blocks, ("shift", "rows")))
    basis = dot_high(mixed, upper_inv)
    return (basis, upper)


def solution(mesh):
    in_specs = (P("shift", "rows", None), P("shift", None))
    out_specs = (P(("rows", "shift"), None), P())
    return jax.shard_map(shards, mesh=mesh, in_specs=in_specs, out_specs=out_specs, check_vma=False)
```

```python
import jax
import jax.numpy as jnp
from jax import lax
from jax.experimental import pallas as pl
from jax.experimental.pallas import tpu as pltpu
from jax.sharding import PartitionSpec as P

HIGHEST = lax.Precision.HIGHEST


def cross_products(left, right):
    return jnp.dot(left.T, right, precision=lax.Precision.HIGH, preferred_element_type=jnp.float32)


def dot_high(a, b):
    return jnp.dot(a, b, precision=lax.Precision.HIGH, preferred_element_type=jnp.float32)


def butterfly_sum(x, axes):
    size = lax.axis_size(axes)
    bit = 1
    while bit < size:
        pairs = [(i, i ^ bit) for i in range(size)]
        x = x + lax.ppermute(x, axes, pairs)
        bit *= 2
    return x


def dot(a, b):
    return jnp.dot(a, b, precision=HIGHEST, preferred_element_type=jnp.float32)


def leaf_factor(a, work):
    del work
    m, width = a.shape
    rows = lax.broadcasted_iota(jnp.int32, (m, width), 0)
    cols = lax.broadcasted_iota(jnp.int32, (m, width), 1)
    current = jnp.where(cols < m, a, (cols - m == rows).astype(jnp.float32))
    row_index = lax.broadcasted_iota(jnp.int32, (m, 1), 0)
    for j in range(m):
        row = current[j:j + 1, :]
        scale = 1.0 / jnp.sqrt(row[:, j:j + 1])
        scaled = row * scale
        coef = jnp.where(row_index > j, current[:, j:j + 1] * scale, 0.0)
        current = jnp.where(row_index == j, scaled, current - coef * scaled)
    upper = jnp.where((cols >= rows) & (cols < m), current, 0.0)
    inverse = jnp.where(cols >= m, current, 0.0)
    return upper, inverse


def factor_half(x, work):
    n = x.shape[0]
    m = n // 2
    cols = lax.broadcasted_iota(jnp.int32, (m, n), 1)
    zeros = jnp.zeros((m, n), jnp.float32)
    r11, l11i_high = leaf_factor(x[:m, :], work)
    l11i = pltpu.roll(l11i_high, m, 1)
    r12 = jnp.where(cols >= m, dot(l11i, x), 0.0)
    r12_full = jnp.concatenate([r12, zeros], axis=0)
    schur_rows = (x - dot(r12_full.T, r12_full))[m:, :]
    r22, l22i_high = leaf_factor(pltpu.roll(schur_rows, m, 1), work)
    upper = jnp.concatenate([r11 + r12, pltpu.roll(r22, m, 1)], axis=0)
    first = jnp.concatenate([l11i, zeros], axis=0)
    second = jnp.concatenate([zeros, l22i_high], axis=0)
    inverse = first + second - dot(dot(second, r12_full.T), first)
    return upper, inverse


def factor_kernel(gram_ref, r_ref, rinv_ref, work):
    h = gram_ref.shape[1]
    g = gram_ref[...]
    packed = g[:h]
    rows = lax.broadcasted_iota(jnp.int32, (h, h), 0)
    cols = lax.broadcasted_iota(jnp.int32, (h, h), 1)
    flipped = packed.T
    g11 = jnp.where(rows <= cols, packed, flipped)
    g22 = jnp.where(rows < cols, flipped, jnp.where(rows > cols, packed, g[2 * h:2 * h + 1]))
    r11, l11i = factor_half(g11, work)
    r12 = dot(l11i, g[h:2 * h])
    schur = g22 - dot(r12.T, r12)
    r22, l22i = factor_half(schur, work)
    r11i = l11i.T
    r22i = l22i.T
    rinv12 = -dot(dot(r11i, r12), r22i)
    zero = jnp.zeros((h, h), jnp.float32)
    r_ref[:h, :h] = r11
    r_ref[:h, h:] = r12
    r_ref[h:, :h] = zero
    r_ref[h:, h:] = r22
    rinv_ref[:h, :h] = r11i
    rinv_ref[:h, h:] = rinv12
    rinv_ref[h:, :h] = zero
    rinv_ref[h:, h:] = r22i


def factor(gram):
    n = 2 * gram.shape[1]
    vmem = pl.BlockSpec(memory_space=pltpu.VMEM)
    return pl.pallas_call(
        factor_kernel,
        out_shape=(jax.ShapeDtypeStruct((n, n), jnp.float32), jax.ShapeDtypeStruct((n, n), jnp.float32)),
        in_specs=[vmem],
        out_specs=(vmem, vmem),
        scratch_shapes=[pltpu.VMEM((n // 4, n // 2), jnp.float32)],
    )(gram)


def swap(x, bit):
    size = lax.axis_size("shift")
    return lax.ppermute(x, "shift", [(i, i ^ bit) for i in range(size)])


def take(x, index, axis):
    return lax.dynamic_index_in_dim(x, index, axis=axis, keepdims=False)


def mix_rows(filtered, weights):
    shift = lax.axis_index("shift")
    low, high = shift % 2, shift // 2
    rows, width = filtered.shape[1], filtered.shape[2]
    block, piece = rows // 4, rows // 8
    scale = weights[0][None, :]

    def part(chunk, half):
        start = chunk * block + half * piece
        values = lax.dynamic_slice_in_dim(filtered[0], start, piece, axis=0)
        return values.astype(jnp.float32) * scale

    forward_x = part(2 * (1 - high) + 1 - low, 0)
    forward_y = part(2 * (1 - high) + 1 - low, 1)
    forward_x, forward_y = lax.optimization_barrier((forward_x, forward_y))
    got_forward_x, got_forward_y = swap(forward_x, 1), swap(forward_y, 2)
    stay_x = part(2 * high + 1 - low, 0)
    stay_y = part(2 * (1 - high) + low, 1)
    stay_x, stay_y = lax.optimization_barrier((stay_x, stay_y))
    got_stay_x, got_stay_y = swap(stay_x, 1), swap(stay_y, 2)
    send_first = part(2 * (1 - high) + low, 0) + got_forward_x
    send_second = part(2 * high + 1 - low, 1) + got_forward_y
    send_first, send_second = lax.optimization_barrier((send_first, send_second))
    got_first, got_second = swap(send_first, 2), swap(send_second, 1)
    first = part(2 * high + low, 0) + got_stay_x + got_first
    second = part(2 * high + low, 1) + got_stay_y + got_second
    return jnp.concatenate([first, second], axis=0)


def shards(filtered, weights):
    if lax.axis_size("shift") == 4:
        mixed = mix_rows(filtered, weights)
    else:
        weighted = filtered[0].astype(jnp.float32) * weights[0][None, :]
        mixed = lax.psum_scatter(weighted, "shift", scatter_dimension=0, tiled=True)
    devices_all = lax.axis_size(("shift", "rows"))
    total_rows = mixed.shape[0] * devices_all
    half = mixed.shape[1] // 2
    top = cross_products(mixed[:, :half], mixed)
    bottom = cross_products(mixed[:, half:], mixed[:, half:])
    rows = lax.broadcasted_iota(jnp.int32, (half, half), 0)
    cols = lax.broadcasted_iota(jnp.int32, (half, half), 1)
    packed = jnp.where(rows <= cols, top[:, :half], bottom.T)
    diagonal = jnp.where(rows[:8] == 0, jnp.sum(jnp.where(rows == cols, bottom, 0.0), axis=0, keepdims=True), 0.0)
    blocks = jnp.concatenate([packed, top[:, half:], diagonal], axis=0) / total_rows
    upper, upper_inv = factor(butterfly_sum(blocks, ("shift", "rows")))
    basis = dot_high(mixed, upper_inv)
    return (basis, upper)


def solution(mesh):
    in_specs = (P("shift", "rows", None), P("shift", None))
    out_specs = (P(("rows", "shift"), None), P())
    return jax.shard_map(shards, mesh=mesh, in_specs=in_specs, out_specs=out_specs, check_vma=False)
```

```python
import jax
import jax.numpy as jnp
from jax import lax
from jax.experimental import pallas as pl
from jax.experimental.pallas import tpu as pltpu
from jax.sharding import PartitionSpec as P

HIGHEST = lax.Precision.HIGHEST


def cross_products(left, right):
    return jnp.dot(left.T, right, precision=lax.Precision.HIGH, preferred_element_type=jnp.float32)


def dot_high(a, b):
    return jnp.dot(a, b, precision=lax.Precision.HIGH, preferred_element_type=jnp.float32)


def butterfly_sum(x, axes):
    size = lax.axis_size(axes)
    bit = 1
    while bit < size:
        pairs = [(i, i ^ bit) for i in range(size)]
        x = x + lax.ppermute(x, axes, pairs)
        bit *= 2
    return x


def dot(a, b):
    return jnp.dot(a, b, precision=HIGHEST, preferred_element_type=jnp.float32)


def leaf_factor(a, work):
    del work
    m, width = a.shape
    rows = lax.broadcasted_iota(jnp.int32, (m, width), 0)
    cols = lax.broadcasted_iota(jnp.int32, (m, width), 1)
    current = jnp.where(cols < m, a, (cols - m == rows).astype(jnp.float32))
    row_index = lax.broadcasted_iota(jnp.int32, (m, 1), 0)
    for j in range(m):
        row = current[j:j + 1, :]
        scale = 1.0 / jnp.sqrt(row[:, j:j + 1])
        scaled = row * scale
        coef = jnp.where(row_index > j, current[:, j:j + 1] * scale, 0.0)
        current = jnp.where(row_index == j, scaled, current - coef * scaled)
    upper = jnp.where((cols >= rows) & (cols < m), current, 0.0)
    inverse = jnp.where(cols >= m, current, 0.0)
    return upper, inverse


def factor_half(x, work):
    n = x.shape[0]
    m = n // 2
    cols = lax.broadcasted_iota(jnp.int32, (m, n), 1)
    zeros = jnp.zeros((m, n), jnp.float32)
    r11, l11i_high = leaf_factor(x[:m, :], work)
    l11i = pltpu.roll(l11i_high, m, 1)
    r12 = jnp.where(cols >= m, dot(l11i, x), 0.0)
    r12_full = jnp.concatenate([r12, zeros], axis=0)
    schur_rows = (x - dot(r12_full.T, r12_full))[m:, :]
    r22, l22i_high = leaf_factor(pltpu.roll(schur_rows, m, 1), work)
    upper = jnp.concatenate([r11 + r12, pltpu.roll(r22, m, 1)], axis=0)
    first = jnp.concatenate([l11i, zeros], axis=0)
    second = jnp.concatenate([zeros, l22i_high], axis=0)
    inverse = first + second - dot(second, dot(r12_full.T, first))
    return upper, inverse


def factor_kernel(gram_ref, r_ref, rinv_ref, work):
    h = gram_ref.shape[1]
    g = gram_ref[...]
    packed = g[:h]
    rows = lax.broadcasted_iota(jnp.int32, (h, h), 0)
    cols = lax.broadcasted_iota(jnp.int32, (h, h), 1)
    flipped = packed.T
    g11 = jnp.where(rows <= cols, packed, flipped)
    g22 = jnp.where(rows < cols, flipped, jnp.where(rows > cols, packed, g[2 * h:2 * h + 1]))
    r11, l11i = factor_half(g11, work)
    r12 = dot(l11i, g[h:2 * h])
    schur = g22 - dot(r12.T, r12)
    r11i = l11i.T
    head = dot(r11i, r12)
    r22, l22i = factor_half(schur, work)
    r22i = l22i.T
    rinv12 = -dot(head, r22i)
    zero = jnp.zeros((h, h), jnp.float32)
    r_ref[:h, :h] = r11
    r_ref[:h, h:] = r12
    r_ref[h:, :h] = zero
    r_ref[h:, h:] = r22
    rinv_ref[:h, :h] = r11i
    rinv_ref[:h, h:] = rinv12
    rinv_ref[h:, :h] = zero
    rinv_ref[h:, h:] = r22i


def factor(gram):
    n = 2 * gram.shape[1]
    vmem = pl.BlockSpec(memory_space=pltpu.VMEM)
    return pl.pallas_call(
        factor_kernel,
        out_shape=(jax.ShapeDtypeStruct((n, n), jnp.float32), jax.ShapeDtypeStruct((n, n), jnp.float32)),
        in_specs=[vmem],
        out_specs=(vmem, vmem),
        scratch_shapes=[pltpu.VMEM((n // 4, n // 2), jnp.float32)],
    )(gram)


def swap(x, bit):
    size = lax.axis_size("shift")
    return lax.ppermute(x, "shift", [(i, i ^ bit) for i in range(size)])


def take(x, index, axis):
    return lax.dynamic_index_in_dim(x, index, axis=axis, keepdims=False)


def mix_rows(filtered, weights):
    shift = lax.axis_index("shift")
    low, high = shift % 2, shift // 2
    rows, width = filtered.shape[1], filtered.shape[2]
    block, piece = rows // 4, rows // 8
    scale = weights[0][None, :]

    def part(chunk, half):
        start = chunk * block + half * piece
        values = lax.dynamic_slice_in_dim(filtered[0], start, piece, axis=0)
        return values.astype(jnp.float32) * scale

    forward_x = part(2 * (1 - high) + 1 - low, 0)
    forward_y = part(2 * (1 - high) + 1 - low, 1)
    forward_x, forward_y = lax.optimization_barrier((forward_x, forward_y))
    got_forward_x, got_forward_y = swap(forward_x, 1), swap(forward_y, 2)
    stay_x = part(2 * high + 1 - low, 0)
    stay_y = part(2 * (1 - high) + low, 1)
    stay_x, stay_y = lax.optimization_barrier((stay_x, stay_y))
    got_stay_x, got_stay_y = swap(stay_x, 1), swap(stay_y, 2)
    send_first = part(2 * (1 - high) + low, 0) + got_forward_x
    send_second = part(2 * high + 1 - low, 1) + got_forward_y
    send_first, send_second = lax.optimization_barrier((send_first, send_second))
    got_first, got_second = swap(send_first, 2), swap(send_second, 1)
    first = part(2 * high + low, 0) + got_stay_x + got_first
    second = part(2 * high + low, 1) + got_stay_y + got_second
    return jnp.concatenate([first, second], axis=0)


def shards(filtered, weights):
    if lax.axis_size("shift") == 4:
        mixed = mix_rows(filtered, weights)
    else:
        weighted = filtered[0].astype(jnp.float32) * weights[0][None, :]
        mixed = lax.psum_scatter(weighted, "shift", scatter_dimension=0, tiled=True)
    devices_all = lax.axis_size(("shift", "rows"))
    total_rows = mixed.shape[0] * devices_all
    half = mixed.shape[1] // 2
    top = cross_products(mixed[:, :half], mixed)
    bottom = cross_products(mixed[:, half:], mixed[:, half:])
    rows = lax.broadcasted_iota(jnp.int32, (half, half), 0)
    cols = lax.broadcasted_iota(jnp.int32, (half, half), 1)
    packed = jnp.where(rows <= cols, top[:, :half], bottom.T)
    diagonal = jnp.where(rows[:8] == 0, jnp.sum(jnp.where(rows == cols, bottom, 0.0), axis=0, keepdims=True), 0.0)
    blocks = jnp.concatenate([packed, top[:, half:], diagonal], axis=0) / total_rows
    upper, upper_inv = factor(butterfly_sum(blocks, ("shift", "rows")))
    basis = dot_high(mixed, upper_inv)
    return (basis, upper)


def solution(mesh):
    in_specs = (P("shift", "rows", None), P("shift", None))
    out_specs = (P(("rows", "shift"), None), P())
    return jax.shard_map(shards, mesh=mesh, in_specs=in_specs, out_specs=out_specs, check_vma=False)
```

```python
import jax
import jax.numpy as jnp
from jax import lax
from jax.experimental import pallas as pl
from jax.experimental.pallas import tpu as pltpu
from jax.sharding import PartitionSpec as P

HIGHEST = lax.Precision.HIGHEST


def cross_products(left, right):
    return jnp.dot(left.T, right, precision=lax.Precision.HIGH, preferred_element_type=jnp.float32)


def dot_high(a, b):
    return jnp.dot(a, b, precision=lax.Precision.HIGH, preferred_element_type=jnp.float32)


def butterfly_sum(x, axes):
    size = lax.axis_size(axes)
    bit = 1
    while bit < size:
        pairs = [(i, i ^ bit) for i in range(size)]
        x = x + lax.ppermute(x, axes, pairs)
        bit *= 2
    return x


def dot(a, b):
    return jnp.dot(a, b, precision=HIGHEST, preferred_element_type=jnp.float32)


def leaf_factor(a, work):
    del work
    m, width = a.shape
    rows = lax.broadcasted_iota(jnp.int32, (m, width), 0)
    cols = lax.broadcasted_iota(jnp.int32, (m, width), 1)
    current = jnp.where(cols < m, a, (cols - m == rows).astype(jnp.float32))
    row_index = lax.broadcasted_iota(jnp.int32, (m, 1), 0)
    for j in range(m):
        row = current[j:j + 1, :]
        scale = lax.rsqrt(row[:, j:j + 1])
        scaled = row * scale
        coef = jnp.where(row_index > j, current[:, j:j + 1] * scale, 0.0)
        current = jnp.where(row_index == j, scaled, current - coef * scaled)
    upper = jnp.where((cols >= rows) & (cols < m), current, 0.0)
    inverse = jnp.where(cols >= m, current, 0.0)
    return upper, inverse


def factor_half(x, work):
    n = x.shape[0]
    m = n // 2
    cols = lax.broadcasted_iota(jnp.int32, (m, n), 1)
    zeros = jnp.zeros((m, n), jnp.float32)
    r11, l11i_high = leaf_factor(x[:m, :], work)
    l11i = pltpu.roll(l11i_high, m, 1)
    r12 = jnp.where(cols >= m, dot(l11i, x), 0.0)
    r12_full = jnp.concatenate([r12, zeros], axis=0)
    schur_rows = (x - dot(r12_full.T, r12_full))[m:, :]
    r22, l22i_high = leaf_factor(pltpu.roll(schur_rows, m, 1), work)
    upper = jnp.concatenate([r11 + r12, pltpu.roll(r22, m, 1)], axis=0)
    first = jnp.concatenate([l11i, zeros], axis=0)
    second = jnp.concatenate([zeros, l22i_high], axis=0)
    inverse = first + second - dot(second, dot(r12_full.T, first))
    return upper, inverse


def factor_kernel(gram_ref, r_ref, rinv_ref, work):
    h = gram_ref.shape[1]
    g = gram_ref[...]
    packed = g[:h]
    rows = lax.broadcasted_iota(jnp.int32, (h, h), 0)
    cols = lax.broadcasted_iota(jnp.int32, (h, h), 1)
    flipped = packed.T
    g11 = jnp.where(rows <= cols, packed, flipped)
    g22 = jnp.where(rows < cols, flipped, jnp.where(rows > cols, packed, g[2 * h:2 * h + 1]))
    r11, l11i = factor_half(g11, work)
    r12 = dot(l11i, g[h:2 * h])
    schur = g22 - dot(r12.T, r12)
    r11i = l11i.T
    head = dot(r11i, r12)
    r22, l22i = factor_half(schur, work)
    r22i = l22i.T
    rinv12 = -dot(head, r22i)
    zero = jnp.zeros((h, h), jnp.float32)
    r_ref[:h, :h] = r11
    r_ref[:h, h:] = r12
    r_ref[h:, :h] = zero
    r_ref[h:, h:] = r22
    rinv_ref[:h, :h] = r11i
    rinv_ref[:h, h:] = rinv12
    rinv_ref[h:, :h] = zero
    rinv_ref[h:, h:] = r22i


def factor(gram):
    n = 2 * gram.shape[1]
    vmem = pl.BlockSpec(memory_space=pltpu.VMEM)
    return pl.pallas_call(
        factor_kernel,
        out_shape=(jax.ShapeDtypeStruct((n, n), jnp.float32), jax.ShapeDtypeStruct((n, n), jnp.float32)),
        in_specs=[vmem],
        out_specs=(vmem, vmem),
        scratch_shapes=[pltpu.VMEM((n // 4, n // 2), jnp.float32)],
    )(gram)


def swap(x, bit):
    size = lax.axis_size("shift")
    return lax.ppermute(x, "shift", [(i, i ^ bit) for i in range(size)])


def take(x, index, axis):
    return lax.dynamic_index_in_dim(x, index, axis=axis, keepdims=False)


def mix_rows(filtered, weights):
    shift = lax.axis_index("shift")
    low, high = shift % 2, shift // 2
    rows, width = filtered.shape[1], filtered.shape[2]
    block, piece = rows // 4, rows // 8
    scale = weights[0][None, :]

    def part(chunk, half):
        start = chunk * block + half * piece
        values = lax.dynamic_slice_in_dim(filtered[0], start, piece, axis=0)
        return values.astype(jnp.float32) * scale

    forward_x = part(2 * (1 - high) + 1 - low, 0)
    forward_y = part(2 * (1 - high) + 1 - low, 1)
    forward_x, forward_y = lax.optimization_barrier((forward_x, forward_y))
    got_forward_x, got_forward_y = swap(forward_x, 1), swap(forward_y, 2)
    stay_x = part(2 * high + 1 - low, 0)
    stay_y = part(2 * (1 - high) + low, 1)
    stay_x, stay_y = lax.optimization_barrier((stay_x, stay_y))
    got_stay_x, got_stay_y = swap(stay_x, 1), swap(stay_y, 2)
    send_first = part(2 * (1 - high) + low, 0) + got_forward_x
    send_second = part(2 * high + 1 - low, 1) + got_forward_y
    send_first, send_second = lax.optimization_barrier((send_first, send_second))
    got_first, got_second = swap(send_first, 2), swap(send_second, 1)
    first = part(2 * high + low, 0) + got_stay_x + got_first
    second = part(2 * high + low, 1) + got_stay_y + got_second
    return jnp.concatenate([first, second], axis=0)


def shards(filtered, weights):
    if lax.axis_size("shift") == 4:
        mixed = mix_rows(filtered, weights)
    else:
        weighted = filtered[0].astype(jnp.float32) * weights[0][None, :]
        mixed = lax.psum_scatter(weighted, "shift", scatter_dimension=0, tiled=True)
    devices_all = lax.axis_size(("shift", "rows"))
    total_rows = mixed.shape[0] * devices_all
    half = mixed.shape[1] // 2
    top = cross_products(mixed[:, :half], mixed)
    bottom = cross_products(mixed[:, half:], mixed[:, half:])
    rows = lax.broadcasted_iota(jnp.int32, (half, half), 0)
    cols = lax.broadcasted_iota(jnp.int32, (half, half), 1)
    packed = jnp.where(rows <= cols, top[:, :half], bottom.T)
    diagonal = jnp.where(rows[:8] == 0, jnp.sum(jnp.where(rows == cols, bottom, 0.0), axis=0, keepdims=True), 0.0)
    blocks = jnp.concatenate([packed, top[:, half:], diagonal], axis=0) / total_rows
    upper, upper_inv = factor(butterfly_sum(blocks, ("shift", "rows")))
    basis = dot_high(mixed, upper_inv)
    return (basis, upper)


def solution(mesh):
    in_specs = (P("shift", "rows", None), P("shift", None))
    out_specs = (P(("rows", "shift"), None), P())
    return jax.shard_map(shards, mesh=mesh, in_specs=in_specs, out_specs=out_specs, check_vma=False)
```
